32 devices in a mesh: segment: 4 (over z), rows: 8 (over y, x, core).
Axes of the slice: x: 2, y: 2, z: 4, core: 2. Of those that a mesh axis runs over, the one named last changes fastest.
Arguments:
- features: bfloat16 [4, 32, 24, 384], P(None, 'rows'), may hold values from -6 to 6
- gains: bfloat16 [4, 384], P('segment'), may hold values from 0.5 to 2
- kernels: bfloat16 [4, 3, 3, 3, 384, 384], P('segment'), may hold values from -0.0625 to 0.0625
Outputs:
- decoded: bfloat16 [4, 32, 24, 384], P('segment', 'rows')
The draws below stay inside these ranges and needn't reach their ends.
All inputs are finite; a program needn't handle non-finite values.
Results may differ from the reference program's by a relative error of at most 0.014.
Values may be sent and summed in bfloat16 or wider, within the bound.
No kernel may reach another device: no remote copies, remote signals or barrier semaphores. Data moves between devices by JAX's collectives and lax.ppermute only.
A program may use at most 64 MiB of HBM per device.

```python
import math
import jax
import jax.numpy as jnp
from jax import lax

C = 384
COLS = 24
SEGMENTS = 4
FRAMES = 4
H = 32


def level_of(rng, dims, pieces, smallest, top_value):
    level = 1.0
    for axis_at, shards_of in pieces:
        heights = jax.random.uniform(jax.random.fold_in(jax.random.fold_in(rng, 6), axis_at), (shards_of,), jnp.float32, smallest / len(pieces), top_value / len(pieces))
        level = level * jnp.repeat(jnp.exp(heights), dims[axis_at] // shards_of).reshape((-1,) + (1,) * (len(dims) - 1 - axis_at))
    return level


def centred(own_key, shape, scale, bound, cuts=(), dtype=jnp.bfloat16):
    level = level_of(own_key, shape, cuts, -0.22, 0.18) if cuts else 1.0
    array = jax.random.normal(own_key, shape, jnp.float32) * scale * level
    return jnp.minimum(jnp.maximum(array, -bound), bound).astype(dtype)


def setup_inputs(seed: int = 0) -> dict:
    keys = jax.random.split(jax.random.key(seed), 4)
    return {
        "features": centred(keys[0], (FRAMES, H, COLS, C), 1.0, 6.0, ((1, 8),)),
        "gains": jnp.clip(jnp.exp(math.log(2.0) - 1.3862944 * jax.random.uniform(keys[1], (SEGMENTS, C), jnp.float32) ** level_of(keys[1], (SEGMENTS, C), ((0, 4),), -0.2, 0.2)), 0.5, 2.0).astype(jnp.bfloat16),
        "kernels": centred(keys[2], (SEGMENTS, 3, 3, 3, C, C), (27 * C) ** -0.5, 0.0625, ((0, 4),)),
    }


def activate(values_in, gain_row):
    widened = values_in.astype(jnp.float32)
    mean_square = lax.optimization_barrier(jnp.mean(widened * widened, axis=-1, keepdims=True))
    return jax.nn.silu(widened * lax.rsqrt(mean_square + 1e-06) * gain_row.astype(jnp.float32)).astype(jnp.bfloat16)

def causal_conv(field_in, kernel):
    frame_count, height, columns, channels = field_in.shape
    padded = jnp.pad(field_in, ((2, 0), (1, 1), (1, 1), (0, 0)))
    tap_list = []
    for time_off in range(3):
        for row_off in range(3):
            for col_off in range(3):
                tap_list.append(padded[time_off:time_off + frame_count, row_off:row_off + height, col_off:col_off + columns])
    stacked = jnp.concatenate(tap_list, axis=-1).reshape(frame_count * height * columns, 27 * channels)
    result = jnp.dot(stacked, kernel.reshape(27 * channels, channels), preferred_element_type=jnp.float32)
    return result.reshape(frame_count, height, columns, channels)

def reference(features, gains, kernels):
    current = features
    for block_index in range(SEGMENTS // 2):
        first = 2 * block_index
        inner_out = causal_conv(activate(current, gains[first]), kernels[first]).astype(jnp.bfloat16)
        branch = causal_conv(activate(inner_out, gains[first + 1]), kernels[first + 1])
        current = (current.astype(jnp.float32) + branch).astype(jnp.bfloat16)
    return current
```

```python
import jax
import jax.numpy as jnp
from jax import lax
from jax.sharding import PartitionSpec as P

BOTH = ("segment", "rows")


def activate(values_in, gain_row):
    widened = values_in.astype(jnp.float32)
    mean_square = jnp.mean(widened * widened, axis=-1, keepdims=True)
    return jax.nn.silu(
        widened * lax.rsqrt(mean_square + 1e-06) * gain_row.astype(jnp.float32)
    ).astype(jnp.bfloat16)


def causal_conv(window, kernel):
    result = lax.conv_general_dilated(
        window[None],
        kernel,
        window_strides=(1, 1, 1),
        padding=((2, 0), (0, 0), (1, 1)),
        dimension_numbers=("NDHWC", "DHWIO", "NDHWC"),
        preferred_element_type=jnp.float32,
    )
    return result[0]


def send(value, pairs):
    return lax.ppermute(value, BOTH, pairs)


def stage_send(value, stage, row_count):
    base, nxt = stage * row_count, (stage + 1) * row_count
    height = value.shape[1]
    body = send(value, [(base + r, nxt + r) for r in range(row_count)])
    top = send(
        value[:, height - 1 :],
        [(base + r, nxt + r + 1) for r in range(row_count - 1)],
    )
    bottom = send(value[:, :1], [(base + r, nxt + r - 1) for r in range(1, row_count)])
    return body, top, bottom


def local(features, gains, kernels):
    segment_count = lax.axis_size("segment")
    row_count = lax.axis_size("rows")
    segment_index = lax.axis_index("segment")
    frame_count, height, columns, channels = features.shape
    gain_row = gains[0]
    kernel = kernels[0]

    up = [(i, i + 1) for i in range(row_count - 1)]
    down = [(i + 1, i) for i in range(row_count - 1)]
    top = lax.ppermute(features[:, height - 1 :], "rows", up)
    bottom = lax.ppermute(features[:, :1], "rows", down)
    current = features
    skip = features

    for stage in range(segment_count):
        window = jnp.concatenate([top, current, bottom], axis=1)
        convolved = causal_conv(activate(window, gain_row), kernel)
        if stage % 2 == 0:
            produced = convolved.astype(jnp.bfloat16)
            next_skip = current
        else:
            produced = (skip.astype(jnp.float32) + convolved).astype(jnp.bfloat16)
            next_skip = None
        if stage == segment_count - 1:
            decoded = produced
            break
        current, top, bottom = stage_send(produced, stage, row_count)
        if next_skip is not None:
            base, nxt = stage * row_count, (stage + 1) * row_count
            skip = send(next_skip, [(base + r, nxt + r) for r in range(row_count)])

    group = frame_count // segment_count
    last = (segment_count - 1) * row_count
    delivered = decoded[(segment_count - 1) * group :]
    for target in range(segment_count - 1):
        piece = send(
            decoded[target * group : (target + 1) * group],
            [(last + r, target * row_count + r) for r in range(row_count)],
        )
        delivered = jnp.where(segment_index == target, piece, delivered)
    return delivered


def solution(mesh):
    placed = (
        P(None, "rows", None, None),
        P("segment", None),
        P("segment", None, None, None, None, None),
    )
    return jax.shard_map(
        local,
        mesh=mesh,
        in_specs=placed,
        out_specs=P("segment", "rows", None, None),
        check_vma=False,
    )
```

```python
import jax
import jax.numpy as jnp
from jax import lax
from jax.sharding import PartitionSpec as P

BOTH = ("segment", "rows")


def activate(values_in, gain_row):
    widened = values_in.astype(jnp.float32)
    mean_square = jnp.mean(widened * widened, axis=-1, keepdims=True)
    return jax.nn.silu(
        widened * lax.rsqrt(mean_square + 1e-06) * gain_row.astype(jnp.float32)
    ).astype(jnp.bfloat16)


def causal_conv(window, kernel):
    result = lax.conv_general_dilated(
        window[None],
        kernel,
        window_strides=(1, 1, 1),
        padding=((2, 0), (0, 0), (1, 1)),
        dimension_numbers=("NDHWC", "DHWIO", "NDHWC"),
        preferred_element_type=jnp.float32,
    )
    return result[0]


def send(value, pairs):
    return lax.ppermute(value, BOTH, pairs)


def stage_send(value, stage, row_count):
    base, nxt = stage * row_count, (stage + 1) * row_count
    height = value.shape[1]
    body = send(value, [(base + r, nxt + r) for r in range(row_count)])
    top = send(
        value[:, height - 1 :],
        [(base + r, nxt + r + 1) for r in range(row_count - 1)],
    )
    bottom = send(value[:, :1], [(base + r, nxt + r - 1) for r in range(1, row_count)])
    return body, top, bottom


def local(features, gains, kernels):
    segment_count = lax.axis_size("segment")
    row_count = lax.axis_size("rows")
    segment_index = lax.axis_index("segment")
    frame_count, height, columns, channels = features.shape
    gain_row = gains[0]
    kernel = kernels[0]

    up = [(i, i + 1) for i in range(row_count - 1)]
    down = [(i + 1, i) for i in range(row_count - 1)]
    top = lax.ppermute(features[:, height - 1 :], "rows", up)
    bottom = lax.ppermute(features[:, :1], "rows", down)
    current = features
    skip = features

    for stage in range(segment_count):
        window = jnp.concatenate([top, current, bottom], axis=1)
        odd = stage % 2 == 1

        def compute(window, skip, odd=odd):
            convolved = causal_conv(activate(window, gain_row), kernel)
            if odd:
                convolved = skip.astype(jnp.float32) + convolved
            return convolved.astype(jnp.bfloat16)

        def idle(window, skip):
            return jnp.zeros(skip.shape, jnp.bfloat16)

        produced = lax.cond(segment_index == stage, compute, idle, window, skip)
        next_skip = None if odd else current
        if stage == segment_count - 1:
            decoded = produced
            break
        current, top, bottom = stage_send(produced, stage, row_count)
        if next_skip is not None:
            base, nxt = stage * row_count, (stage + 1) * row_count
            skip = send(next_skip, [(base + r, nxt + r) for r in range(row_count)])

    group = frame_count // segment_count
    last = (segment_count - 1) * row_count
    delivered = decoded[(segment_count - 1) * group :]
    for target in range(segment_count - 1):
        piece = send(
            decoded[target * group : (target + 1) * group],
            [(last + r, target * row_count + r) for r in range(row_count)],
        )
        delivered = jnp.where(segment_index == target, piece, delivered)
    return delivered


def solution(mesh):
    placed = (
        P(None, "rows", None, None),
        P("segment", None),
        P("segment", None, None, None, None, None),
    )
    return jax.shard_map(
        local,
        mesh=mesh,
        in_specs=placed,
        out_specs=P("segment", "rows", None, None),
        check_vma=False,
    )
```

```python
import jax
import jax.numpy as jnp
from jax import lax
from jax.sharding import PartitionSpec as P

BOTH = ("segment", "rows")


def activate(values_in, gain_row):
    widened = values_in.astype(jnp.float32)
    mean_square = jnp.mean(widened * widened, axis=-1, keepdims=True)
    return jax.nn.silu(
        widened * lax.rsqrt(mean_square + 1e-06) * gain_row.astype(jnp.float32)
    ).astype(jnp.bfloat16)


def causal_conv(window, kernel):
    result = lax.conv_general_dilated(
        window[None],
        kernel,
        window_strides=(1, 1, 1),
        padding=((2, 0), (0, 0), (1, 1)),
        dimension_numbers=("NDHWC", "DHWIO", "NDHWC"),
        preferred_element_type=jnp.float32,
    )
    return result[0]


def send(value, pairs):
    return lax.ppermute(value, BOTH, pairs)


def stage_send(value, stage, row_count):
    base, nxt = stage * row_count, (stage + 1) * row_count
    height = value.shape[1]
    body = send(value, [(base + r, nxt + r) for r in range(row_count)])
    top = send(
        value[:, height - 1 :],
        [(base + r, nxt + r + 1) for r in range(row_count - 1)],
    )
    bottom = send(value[:, :1], [(base + r, nxt + r - 1) for r in range(1, row_count)])
    return body, top, bottom


def local(features, gains, kernels):
    segment_count = lax.axis_size("segment")
    row_count = lax.axis_size("rows")
    segment_index = lax.axis_index("segment")
    frame_count, height, columns, channels = features.shape
    group = frame_count // segment_count
    gain_row = gains[0]
    kernel = kernels[0]

    def straight(source, target):
        return [(source * row_count + r, target * row_count + r) for r in range(row_count)]

    up = [(i, i + 1) for i in range(row_count - 1)]
    down = [(i + 1, i) for i in range(row_count - 1)]
    top = lax.ppermute(features[:, height - 1 :], "rows", up)
    bottom = lax.ppermute(features[:, :1], "rows", down)
    current = features
    skip = features
    last_stage = segment_count - 1

    for stage in range(segment_count):
        window = jnp.concatenate([top, current, bottom], axis=1)
        odd = stage % 2 == 1
        final = stage == last_stage

        def compute(window, skip, odd=odd, final=final):
            convolved = causal_conv(activate(window, gain_row), kernel)
            if final:
                return convolved
            if odd:
                convolved = skip.astype(jnp.float32) + convolved
            return convolved.astype(jnp.bfloat16)

        def idle(window, skip, final=final):
            return jnp.zeros(skip.shape, jnp.float32 if final else jnp.bfloat16)

        produced = lax.cond(segment_index == stage, compute, idle, window, skip)
        if final:
            break
        if stage == last_stage - 1:
            owned = current[stage * group : (stage + 1) * group]
            for target in range(segment_count):
                chunk = current[target * group : (target + 1) * group]
                if stage == 0:
                    owned = jnp.where(segment_index == target, chunk, owned)
                elif target != stage:
                    piece = send(chunk, straight(stage, target))
                    owned = jnp.where(segment_index == target, piece, owned)
        next_skip = current if (not odd and stage > 0 and stage != last_stage - 1) else None
        current, top, bottom = stage_send(produced, stage, row_count)
        if next_skip is not None:
            skip = send(next_skip, straight(stage, stage + 1))
        elif not odd:
            skip = features

    branch = produced[last_stage * group :]
    for target in range(last_stage):
        piece = send(
            produced[target * group : (target + 1) * group].astype(jnp.bfloat16),
            straight(last_stage, target),
        )
        branch = jnp.where(segment_index == target, piece.astype(jnp.float32), branch)
    return (owned.astype(jnp.float32) + branch).astype(jnp.bfloat16)


def solution(mesh):
    placed = (
        P(None, "rows", None, None),
        P("segment", None),
        P("segment", None, None, None, None, None),
    )
    return jax.shard_map(
        local,
        mesh=mesh,
        in_specs=placed,
        out_specs=P("segment", "rows", None, None),
        check_vma=False,
    )
```

```python
import jax
import jax.numpy as jnp
from jax import lax
from jax.sharding import PartitionSpec as P

BOTH = ("segment", "rows")


def activate(values_in, gain_row):
    widened = values_in.astype(jnp.float32)
    mean_square = jnp.mean(widened * widened, axis=-1, keepdims=True)
    return jax.nn.silu(
        widened * lax.rsqrt(mean_square + 1e-06) * gain_row.astype(jnp.float32)
    ).astype(jnp.bfloat16)


def causal_conv(window, kernel):
    result = lax.conv_general_dilated(
        window[None],
        kernel,
        window_strides=(1, 1, 1),
        padding=((2, 0), (0, 0), (1, 1)),
        dimension_numbers=("NDHWC", "DHWIO", "NDHWC"),
        preferred_element_type=jnp.float32,
    )
    return result[0]


def send(value, pairs):
    return lax.ppermute(value, BOTH, pairs)


def stage_send(value, stage, row_count):
    base, nxt = stage * row_count, (stage + 1) * row_count
    height = value.shape[1]
    body = send(value, [(base + r, nxt + r) for r in range(row_count)])
    top = send(
        value[:, height - 1 :],
        [(base + r, nxt + r + 1) for r in range(row_count - 1)],
    )
    bottom = send(value[:, :1], [(base + r, nxt + r - 1) for r in range(1, row_count)])
    return body, top, bottom


def local(features, gains, kernels):
    segment_count = lax.axis_size("segment")
    row_count = lax.axis_size("rows")
    segment_index = lax.axis_index("segment")
    frame_count, height, columns, channels = features.shape
    group = frame_count // segment_count
    gain_row = gains[0]
    kernel = kernels[0]

    def straight(source, target):
        return [(source * row_count + r, target * row_count + r) for r in range(row_count)]

    up = [(i, i + 1) for i in range(row_count - 1)]
    down = [(i + 1, i) for i in range(row_count - 1)]
    top = lax.ppermute(features[:, height - 1 :], "rows", up)
    bottom = lax.ppermute(features[:, :1], "rows", down)
    current = features
    skip = features
    last_stage = segment_count - 1

    for stage in range(segment_count):
        window = jnp.concatenate([top, current, bottom], axis=1)
        odd = stage % 2 == 1
        final = stage == last_stage

        def compute(window, skip, odd=odd, final=final):
            convolved = causal_conv(activate(window, gain_row), kernel).astype(jnp.bfloat16)
            if odd and not final:
                convolved = (skip.astype(jnp.float32) + convolved).astype(jnp.bfloat16)
            return convolved

        def idle(window, skip):
            return jnp.zeros(skip.shape, jnp.bfloat16)

        produced = lax.cond(segment_index == stage, compute, idle, window, skip)
        if final:
            break
        if stage == last_stage - 1:
            owned = current[stage * group : (stage + 1) * group]
            for target in range(segment_count):
                chunk = current[target * group : (target + 1) * group]
                if stage == 0:
                    owned = jnp.where(segment_index == target, chunk, owned)
                elif target != stage:
                    piece = send(chunk, straight(stage, target))
                    owned = jnp.where(segment_index == target, piece, owned)
        next_skip = current if (not odd and stage > 0 and stage != last_stage - 1) else None
        current, top, bottom = stage_send(produced, stage, row_count)
        if next_skip is not None:
            skip = send(next_skip, straight(stage, stage + 1))
        elif not odd:
            skip = features

    branch = produced[last_stage * group :]
    for target in range(last_stage):
        chunk = produced[target * group : (target + 1) * group]
        piece = send(chunk, straight(last_stage, target))
        branch = jnp.where(segment_index == target, piece, branch)
    return (owned.astype(jnp.float32) + branch.astype(jnp.float32)).astype(jnp.bfloat16)


def solution(mesh):
    placed = (
        P(None, "rows", None, None),
        P("segment", None),
        P("segment", None, None, None, None, None),
    )
    return jax.shard_map(
        local,
        mesh=mesh,
        in_specs=placed,
        out_specs=P("segment", "rows", None, None),
        check_vma=False,
    )
```

```python
import jax
import jax.numpy as jnp
from jax import lax
from jax.sharding import PartitionSpec as P

BOTH = ("segment", "rows")


def activate(values_in, gain_row):
    widened = values_in.astype(jnp.float32)
    mean_square = jnp.mean(widened * widened, axis=-1, keepdims=True)
    return jax.nn.silu(
        widened * lax.rsqrt(mean_square + 1e-06) * gain_row.astype(jnp.float32)
    ).astype(jnp.bfloat16)


def causal_conv(window, kernel):
    result = lax.conv_general_dilated(
        window[None],
        kernel,
        window_strides=(1, 1, 1),
        padding=((2, 0), (0, 0), (1, 1)),
        dimension_numbers=("NDHWC", "DHWIO", "NDHWC"),
        preferred_element_type=jnp.float32,
    )
    return result[0]


def send(value, pairs):
    return lax.ppermute(value, BOTH, pairs)


def local(features, gains, kernels):
    segment_count = lax.axis_size("segment")
    row_count = lax.axis_size("rows")
    segment_index = lax.axis_index("segment")
    frame_count, height, columns, channels = features.shape
    size = 2 if frame_count % 2 == 0 else 1
    groups = frame_count // size
    owned_frames = frame_count // segment_count
    last = segment_count - 1
    gain_row = gains[0]
    kernel = kernels[0]

    def straight(source, target):
        return [(source * row_count + r, target * row_count + r) for r in range(row_count)]

    senders = range(segment_count - 1)
    body_pairs = [p for k in senders for p in straight(k, k + 1)]
    top_pairs = [
        (k * row_count + r, (k + 1) * row_count + r + 1)
        for k in senders
        for r in range(row_count - 1)
    ]
    bottom_pairs = [
        (k * row_count + r, (k + 1) * row_count + r - 1)
        for k in senders
        for r in range(1, row_count)
    ]
    skip_pairs = [p for k in range(2, segment_count - 2, 2) for p in straight(k, k + 1)]

    up = [(i, i + 1) for i in range(row_count - 1)]
    down = [(i + 1, i) for i in range(row_count - 1)]
    features_top = lax.ppermute(features[:, height - 1 :], "rows", up)
    features_bottom = lax.ppermute(features[:, :1], "rows", down)

    body_in = jnp.zeros((size, height, columns, channels), jnp.bfloat16)
    top_in = jnp.zeros((size, 1, columns, channels), jnp.bfloat16)
    bottom_in = top_in
    skip_in = body_in
    cache = jnp.zeros((2, height + 2, columns, channels), jnp.bfloat16)
    decoded = jnp.zeros(features.shape, jnp.bfloat16)
    block_input = jnp.zeros(features.shape, jnp.bfloat16)
    first_stage = segment_index == 0
    adds_skip = jnp.logical_and(segment_index % 2 == 1, segment_index != last)

    wavefronts = segment_count + groups - 1
    for wave in range(wavefronts):
        group = wave - segment_index
        valid = jnp.logical_and(group >= 0, group < groups)
        start = jnp.clip(group, 0, groups - 1) * size
        local_body = lax.dynamic_slice_in_dim(features, start, size, 0)
        body = jnp.where(first_stage, local_body, body_in)
        top = jnp.where(
            first_stage, lax.dynamic_slice_in_dim(features_top, start, size, 0), top_in
        )
        bottom = jnp.where(
            first_stage, lax.dynamic_slice_in_dim(features_bottom, start, size, 0), bottom_in
        )
        window = activate(jnp.concatenate([top, body, bottom], axis=1), gain_row)
        full = jnp.concatenate([cache, window], axis=0)
        convolved = lax.conv_general_dilated(
            full[None],
            kernel,
            window_strides=(1, 1, 1),
            padding=((0, 0), (0, 0), (1, 1)),
            dimension_numbers=("NDHWC", "DHWIO", "NDHWC"),
            preferred_element_type=jnp.float32,
        )[0].astype(jnp.bfloat16)
        skip = jnp.where(segment_index == 1, local_body, skip_in)
        summed = (skip.astype(jnp.float32) + convolved.astype(jnp.float32)).astype(
            jnp.bfloat16
        )
        produced = jnp.where(adds_skip, summed, convolved)
        cache = jnp.where(valid, full[size:], cache)
        decoded = jnp.where(
            jnp.logical_and(valid, segment_index == last),
            lax.dynamic_update_slice_in_dim(decoded, produced, start, 0),
            decoded,
        )
        block_input = jnp.where(
            jnp.logical_and(valid, segment_index == last - 1),
            lax.dynamic_update_slice_in_dim(block_input, body, start, 0),
            block_input,
        )
        if wave < wavefronts - 1:
            body_in = send(produced, body_pairs)
            top_in = send(produced[:, height - 1 :], top_pairs)
            bottom_in = send(produced[:, :1], bottom_pairs)
            if skip_pairs:
                skip_in = send(body, skip_pairs)

    def frames_of(array, target):
        return array[target * owned_frames : (target + 1) * owned_frames]

    held_input = frames_of(block_input, last - 1)
    held_branch = frames_of(decoded, last)
    for target in range(segment_count):
        if target != last - 1:
            piece = send(frames_of(block_input, target), straight(last - 1, target))
            held_input = jnp.where(segment_index == target, piece, held_input)
        if target != last:
            piece = send(frames_of(decoded, target), straight(last, target))
            held_branch = jnp.where(segment_index == target, piece, held_branch)
    return (held_input.astype(jnp.float32) + held_branch.astype(jnp.float32)).astype(
        jnp.bfloat16
    )


def solution(mesh):
    placed = (
        P(None, "rows", None, None),
        P("segment", None),
        P("segment", None, None, None, None, None),
    )
    return jax.shard_map(
        local,
        mesh=mesh,
        in_specs=placed,
        out_specs=P("segment", "rows", None, None),
        check_vma=False,
    )
```

```python
import jax
import jax.numpy as jnp
from jax import lax
from jax.sharding import PartitionSpec as P

BOTH = ("segment", "rows")


def activate(values_in, gain_row):
    widened = values_in.astype(jnp.float32)
    mean_square = jnp.mean(widened * widened, axis=-1, keepdims=True)
    return jax.nn.silu(
        widened * lax.rsqrt(mean_square + 1e-06) * gain_row.astype(jnp.float32)
    ).astype(jnp.bfloat16)


def causal_conv(window, kernel, before=2):
    result = lax.conv_general_dilated(
        window[None],
        kernel,
        window_strides=(1, 1, 1),
        padding=((before, 0), (0, 0), (1, 1)),
        dimension_numbers=("NDHWC", "DHWIO", "NDHWC"),
        preferred_element_type=jnp.float32,
    )
    return result[0]


def send(value, pairs):
    return lax.ppermute(value, BOTH, pairs)


def stage_send(value, stage, row_count):
    base, nxt = stage * row_count, (stage + 1) * row_count
    height = value.shape[1]
    body = send(value, [(base + r, nxt + r) for r in range(row_count)])
    top = send(
        value[:, height - 1 :],
        [(base + r, nxt + r + 1) for r in range(row_count - 1)],
    )
    bottom = send(value[:, :1], [(base + r, nxt + r - 1) for r in range(1, row_count)])
    return body, top, bottom


def local(features, gains, kernels):
    segment_count = lax.axis_size("segment")
    row_count = lax.axis_size("rows")
    segment_index = lax.axis_index("segment")
    frame_count, height, columns, channels = features.shape
    group = frame_count // segment_count
    gain_row = gains[0]
    kernel = kernels[0]

    def straight(source, target):
        return [(source * row_count + r, target * row_count + r) for r in range(row_count)]

    up = [(i, i + 1) for i in range(row_count - 1)]
    down = [(i + 1, i) for i in range(row_count - 1)]
    top = lax.ppermute(features[:, height - 1 :], "rows", up)
    bottom = lax.ppermute(features[:, :1], "rows", down)
    current = features
    skip = features
    last_stage = segment_count - 1

    for stage in range(segment_count):
        window = jnp.concatenate([top, current, bottom], axis=1)
        odd = stage % 2 == 1
        final = stage == last_stage

        def compute(window, skip, odd=odd, final=final):
            convolved = causal_conv(activate(window, gain_row), kernel).astype(jnp.bfloat16)
            if odd and not final:
                convolved = (skip.astype(jnp.float32) + convolved).astype(jnp.bfloat16)
            return convolved

        def idle(window, skip):
            return jnp.zeros(skip.shape, jnp.bfloat16)

        if final:
            activated = jnp.pad(activate(window, gain_row), ((2, 0), (0, 0), (0, 0), (0, 0)))
            split = (segment_count // 2) * group
            branch = None
            for low, high in ((0, split), (split, frame_count)):
                part = causal_conv(activated[low : high + 2], kernel, 0).astype(jnp.bfloat16)
                for target in range(low // group, high // group):
                    chunk = part[target * group - low : (target + 1) * group - low]
                    if target == last_stage:
                        branch = chunk if branch is None else jnp.where(
                            segment_index == target, chunk, branch
                        )
                    else:
                        piece = send(chunk, straight(last_stage, target))
                        branch = piece if branch is None else jnp.where(
                            segment_index == target, piece, branch
                        )
            break
        produced = lax.cond(segment_index == stage, compute, idle, window, skip)
        if stage == last_stage - 1:
            owned = current[stage * group : (stage + 1) * group]
            for target in range(segment_count):
                chunk = current[target * group : (target + 1) * group]
                if stage == 0:
                    owned = jnp.where(segment_index == target, chunk, owned)
                elif target != stage:
                    piece = send(chunk, straight(stage, target))
                    owned = jnp.where(segment_index == target, piece, owned)
        next_skip = current if (not odd and stage > 0 and stage != last_stage - 1) else None
        current, top, bottom = stage_send(produced, stage, row_count)
        if next_skip is not None:
            skip = send(next_skip, straight(stage, stage + 1))
        elif not odd:
            skip = features

    return (owned.astype(jnp.float32) + branch.astype(jnp.float32)).astype(jnp.bfloat16)


def solution(mesh):
    placed = (
        P(None, "rows", None, None),
        P("segment", None),
        P("segment", None, None, None, None, None),
    )
    return jax.shard_map(
        local,
        mesh=mesh,
        in_specs=placed,
        out_specs=P("segment", "rows", None, None),
        check_vma=False,
    )
```

```python
import jax
import jax.numpy as jnp
from jax import lax
from jax.sharding import PartitionSpec as P

BOTH = ("segment", "rows")


def activate(values_in, gain_row):
    widened = values_in.astype(jnp.float32)
    mean_square = jnp.mean(widened * widened, axis=-1, keepdims=True)
    return jax.nn.silu(
        widened * lax.rsqrt(mean_square + 1e-06) * gain_row.astype(jnp.float32)
    ).astype(jnp.bfloat16)


def causal_conv(window, kernel, before=2):
    return batched_conv(window[None], kernel, before)[0]


def batched_conv(windows, kernel, before=2):
    return lax.conv_general_dilated(
        windows,
        kernel,
        window_strides=(1, 1, 1),
        padding=((before, 0), (0, 0), (1, 1)),
        dimension_numbers=("NDHWC", "DHWIO", "NDHWC"),
        preferred_element_type=jnp.float32,
    )


def send(value, pairs):
    return lax.ppermute(value, BOTH, pairs)


def stage_send(value, stage, row_count):
    base, nxt = stage * row_count, (stage + 1) * row_count
    height = value.shape[1]
    body = send(value, [(base + r, nxt + r) for r in range(row_count)])
    top = send(
        value[:, height - 1 :],
        [(base + r, nxt + r + 1) for r in range(row_count - 1)],
    )
    bottom = send(value[:, :1], [(base + r, nxt + r - 1) for r in range(1, row_count)])
    return body, top, bottom


def local(features, gains, kernels):
    segment_count = lax.axis_size("segment")
    row_count = lax.axis_size("rows")
    segment_index = lax.axis_index("segment")
    frame_count, height, columns, channels = features.shape
    group = frame_count // segment_count
    gain_row = gains[0]
    kernel = kernels[0]

    def straight(source, target):
        return [(source * row_count + r, target * row_count + r) for r in range(row_count)]

    up = [(i, i + 1) for i in range(row_count - 1)]
    down = [(i + 1, i) for i in range(row_count - 1)]
    top = lax.ppermute(features[:, height - 1 :], "rows", up)
    bottom = lax.ppermute(features[:, :1], "rows", down)
    current = features
    skip = features
    last_stage = segment_count - 1

    for stage in range(segment_count):
        window = jnp.concatenate([top, current, bottom], axis=1)
        odd = stage % 2 == 1
        final = stage == last_stage

        def compute(window, skip, odd=odd, final=final):
            convolved = causal_conv(activate(window, gain_row), kernel).astype(jnp.bfloat16)
            if odd and not final:
                convolved = (skip.astype(jnp.float32) + convolved).astype(jnp.bfloat16)
            return convolved

        def idle(window, skip):
            return jnp.zeros(skip.shape, jnp.bfloat16)

        if final:
            activated = jnp.pad(activate(window, gain_row), ((2, 0), (0, 0), (0, 0), (0, 0)))
            split = (segment_count // 2) * group
            branch = None
            for low, high in ((0, split), (split, frame_count)):
                part = causal_conv(activated[low : high + 2], kernel, 0).astype(jnp.bfloat16)
                for target in range(low // group, high // group):
                    chunk = part[target * group - low : (target + 1) * group - low]
                    if target == last_stage:
                        branch = chunk if branch is None else jnp.where(
                            segment_index == target, chunk, branch
                        )
                    else:
                        piece = send(chunk, straight(last_stage, target))
                        branch = piece if branch is None else jnp.where(
                            segment_index == target, piece, branch
                        )
            break
        if stage == 0 and height >= 3:
            inner = activate(features, gain_row)
            middle = causal_conv(inner, kernel)
            edges = jnp.stack(
                [
                    jnp.concatenate([activate(top, gain_row), inner[:, :2]], axis=1),
                    jnp.concatenate([inner[:, height - 2 :], activate(bottom, gain_row)], axis=1),
                ]
            )
            rims = batched_conv(edges, kernel)
            produced = jnp.concatenate([rims[0], middle, rims[1]], axis=1).astype(jnp.bfloat16)
        else:
            produced = lax.cond(segment_index == stage, compute, idle, window, skip)
        if stage == last_stage - 1:
            owned = current[stage * group : (stage + 1) * group]
            for target in range(segment_count):
                chunk = current[target * group : (target + 1) * group]
                if stage == 0:
                    owned = jnp.where(segment_index == target, chunk, owned)
                elif target != stage:
                    piece = send(chunk, straight(stage, target))
                    owned = jnp.where(segment_index == target, piece, owned)
        next_skip = current if (not odd and stage > 0 and stage != last_stage - 1) else None
        current, top, bottom = stage_send(produced, stage, row_count)
        if next_skip is not None:
            skip = send(next_skip, straight(stage, stage + 1))
        elif not odd:
            skip = features

    return (owned.astype(jnp.float32) + branch.astype(jnp.float32)).astype(jnp.bfloat16)


def solution(mesh):
    placed = (
        P(None, "rows", None, None),
        P("segment", None),
        P("segment", None, None, None, None, None),
    )
    return jax.shard_map(
        local,
        mesh=mesh,
        in_specs=placed,
        out_specs=P("segment", "rows", None, None),
        check_vma=False,
    )
```

```python
import jax
import jax.numpy as jnp
from jax import lax
from jax.sharding import PartitionSpec as P

BOTH = ("segment", "rows")


def activate(values_in, gain_row):
    widened = values_in.astype(jnp.float32)
    mean_square = jnp.mean(widened * widened, axis=-1, keepdims=True)
    return jax.nn.silu(
        widened * lax.rsqrt(mean_square + 1e-06) * gain_row.astype(jnp.float32)
    ).astype(jnp.bfloat16)


def causal_conv(window, kernel, before=2):
    return batched_conv(window[None], kernel, before)[0]


def batched_conv(windows, kernel, before=2):
    return lax.conv_general_dilated(
        windows,
        kernel,
        window_strides=(1, 1, 1),
        padding=((before, 0), (0, 0), (1, 1)),
        dimension_numbers=("NDHWC", "DHWIO", "NDHWC"),
        preferred_element_type=jnp.float32,
    )


def send(value, pairs):
    return lax.ppermute(value, BOTH, pairs)


def stage_send(value, stage, row_count):
    base, nxt = stage * row_count, (stage + 1) * row_count
    height = value.shape[1]
    body = send(value, [(base + r, nxt + r) for r in range(row_count)])
    top = send(
        value[:, height - 1 :],
        [(base + r, nxt + r + 1) for r in range(row_count - 1)],
    )
    bottom = send(value[:, :1], [(base + r, nxt + r - 1) for r in range(1, row_count)])
    return body, top, bottom


def local(features, gains, kernels):
    segment_count = lax.axis_size("segment")
    row_count = lax.axis_size("rows")
    segment_index = lax.axis_index("segment")
    frame_count, height, columns, channels = features.shape
    group = frame_count // segment_count
    gain_row = gains[0]
    kernel = kernels[0]

    def straight(source, target):
        return [(source * row_count + r, target * row_count + r) for r in range(row_count)]

    up = [(i, i + 1) for i in range(row_count - 1)]
    down = [(i + 1, i) for i in range(row_count - 1)]
    top = lax.ppermute(features[:, height - 1 :], "rows", up)
    bottom = lax.ppermute(features[:, :1], "rows", down)
    current = features
    skip = features
    last_stage = segment_count - 1

    for stage in range(segment_count):
        window = jnp.concatenate([top, current, bottom], axis=1)
        odd = stage % 2 == 1
        final = stage == last_stage

        def compute(window, skip, odd=odd, final=final):
            activated = jnp.pad(activate(window, gain_row), ((2, 0), (0, 0), (0, 0), (0, 0)))
            split = frame_count // 2
            bounds = ((0, split), (split, frame_count)) if split else ((0, frame_count),)
            halves = jnp.stack([activated[low : high + 2] for low, high in bounds])
            convolved = batched_conv(halves, kernel, 0).astype(jnp.bfloat16)
            convolved = convolved.reshape((-1,) + convolved.shape[2:])
            if odd and not final:
                convolved = (skip.astype(jnp.float32) + convolved).astype(jnp.bfloat16)
            return convolved

        def idle(window, skip):
            return jnp.zeros(skip.shape, jnp.bfloat16)

        if final:
            activated = jnp.pad(activate(window, gain_row), ((2, 0), (0, 0), (0, 0), (0, 0)))
            split = (segment_count // 2) * group
            branch = None
            for low, high in ((0, split), (split, frame_count)):
                part = causal_conv(activated[low : high + 2], kernel, 0).astype(jnp.bfloat16)
                for target in range(low // group, high // group):
                    chunk = part[target * group - low : (target + 1) * group - low]
                    if target == last_stage:
                        branch = chunk if branch is None else jnp.where(
                            segment_index == target, chunk, branch
                        )
                    else:
                        piece = send(chunk, straight(last_stage, target))
                        branch = piece if branch is None else jnp.where(
                            segment_index == target, piece, branch
                        )
            break
        produced = lax.cond(segment_index == stage, compute, idle, window, skip)
        if stage == last_stage - 1:
            owned = current[stage * group : (stage + 1) * group]
            for target in range(segment_count):
                chunk = current[target * group : (target + 1) * group]
                if stage == 0:
                    owned = jnp.where(segment_index == target, chunk, owned)
                elif target != stage:
                    piece = send(chunk, straight(stage, target))
                    owned = jnp.where(segment_index == target, piece, owned)
        next_skip = current if (not odd and stage > 0 and stage != last_stage - 1) else None
        current, top, bottom = stage_send(produced, stage, row_count)
        if next_skip is not None:
            skip = send(next_skip, straight(stage, stage + 1))
        elif not odd:
            skip = features

    return (owned.astype(jnp.float32) + branch.astype(jnp.float32)).astype(jnp.bfloat16)


def solution(mesh):
    placed = (
        P(None, "rows", None, None),
        P("segment", None),
        P("segment", None, None, None, None, None),
    )
    return jax.shard_map(
        local,
        mesh=mesh,
        in_specs=placed,
        out_specs=P("segment", "rows", None, None),
        check_vma=False,
    )
```

```python
import jax
import jax.numpy as jnp
from jax import lax
from jax.sharding import PartitionSpec as P

BOTH = ("segment", "rows")


def activate(values_in, gain_row):
    widened = values_in.astype(jnp.float32)
    mean_square = jnp.mean(widened * widened, axis=-1, keepdims=True)
    return jax.nn.silu(
        widened * lax.rsqrt(mean_square + 1e-06) * gain_row.astype(jnp.float32)
    ).astype(jnp.bfloat16)


def causal_conv(window, kernel, before=2):
    result = lax.conv_general_dilated(
        window[None],
        kernel,
        window_strides=(1, 1, 1),
        padding=((before, 0), (0, 0), (1, 1)),
        dimension_numbers=("NDHWC", "DHWIO", "NDHWC"),
        preferred_element_type=jnp.float32,
    )
    return result[0]


def send(value, pairs):
    return lax.ppermute(value, BOTH, pairs)


def stage_send(value, stage, row_count):
    base, nxt = stage * row_count, (stage + 1) * row_count
    height = value.shape[1]
    body = send(value, [(base + r, nxt + r) for r in range(row_count)])
    top = send(
        value[:, height - 1 :],
        [(base + r, nxt + r + 1) for r in range(row_count - 1)],
    )
    bottom = send(value[:, :1], [(base + r, nxt + r - 1) for r in range(1, row_count)])
    return body, top, bottom


def local(features, gains, kernels):
    segment_count = lax.axis_size("segment")
    row_count = lax.axis_size("rows")
    segment_index = lax.axis_index("segment")
    frame_count, height, columns, channels = features.shape
    group = frame_count // segment_count
    gain_row = gains[0]
    kernel = kernels[0]

    def straight(source, target):
        return [(source * row_count + r, target * row_count + r) for r in range(row_count)]

    up = [(i, i + 1) for i in range(row_count - 1)]
    down = [(i + 1, i) for i in range(row_count - 1)]
    top = lax.ppermute(features[:, height - 1 :], "rows", up)
    bottom = lax.ppermute(features[:, :1], "rows", down)
    current = features
    skip = features
    last_stage = segment_count - 1

    for stage in range(segment_count):
        window = jnp.concatenate([top, current, bottom], axis=1)
        odd = stage % 2 == 1
        final = stage == last_stage

        def compute(window, skip, odd=odd, final=final):
            convolved = causal_conv(activate(window, gain_row), kernel).astype(jnp.bfloat16)
            if odd and not final:
                convolved = (skip.astype(jnp.float32) + convolved).astype(jnp.bfloat16)
            return convolved

        if final:
            activated = jnp.pad(activate(window, gain_row), ((2, 0), (0, 0), (0, 0), (0, 0)))
            split = (segment_count // 2) * group
            branch = None
            for low, high in ((0, split), (split, frame_count)):
                part = causal_conv(activated[low : high + 2], kernel, 0).astype(jnp.bfloat16)
                for target in range(low // group, high // group):
                    chunk = part[target * group - low : (target + 1) * group - low]
                    if target == last_stage:
                        branch = chunk if branch is None else jnp.where(
                            segment_index == target, chunk, branch
                        )
                    else:
                        piece = send(chunk, straight(last_stage, target))
                        branch = piece if branch is None else jnp.where(
                            segment_index == target, piece, branch
                        )
            break
        produced = compute(window, skip)
        if stage == last_stage - 1:
            owned = current[stage * group : (stage + 1) * group]
            for target in range(segment_count):
                chunk = current[target * group : (target + 1) * group]
                if stage == 0:
                    owned = jnp.where(segment_index == target, chunk, owned)
                elif target != stage:
                    piece = send(chunk, straight(stage, target))
                    owned = jnp.where(segment_index == target, piece, owned)
        next_skip = current if (not odd and stage > 0 and stage != last_stage - 1) else None
        current, top, bottom = stage_send(produced, stage, row_count)
        if next_skip is not None:
            skip = send(next_skip, straight(stage, stage + 1))
        elif not odd:
            skip = features

    return (owned.astype(jnp.float32) + branch.astype(jnp.float32)).astype(jnp.bfloat16)


def solution(mesh):
    placed = (
        P(None, "rows", None, None),
        P("segment", None),
        P("segment", None, None, None, None, None),
    )
    return jax.shard_map(
        local,
        mesh=mesh,
        in_specs=placed,
        out_specs=P("segment", "rows", None, None),
        check_vma=False,
    )
```

```python
import jax
import jax.numpy as jnp
from jax import lax
from jax.sharding import PartitionSpec as P

BOTH = ("segment", "rows")


def activate(values_in, gain_row):
    widened = values_in.astype(jnp.float32)
    mean_square = jnp.mean(widened * widened, axis=-1, keepdims=True)
    return jax.nn.silu(
        widened * lax.rsqrt(mean_square + 1e-06) * gain_row.astype(jnp.float32)
    ).astype(jnp.bfloat16)


def causal_conv(window, kernel, before=2):
    result = lax.conv_general_dilated(
        window[None],
        kernel,
        window_strides=(1, 1, 1),
        padding=((before, 0), (0, 0), (1, 1)),
        dimension_numbers=("NDHWC", "DHWIO", "NDHWC"),
        preferred_element_type=jnp.float32,
    )
    return result[0]


def send(value, pairs):
    return lax.ppermute(value, BOTH, pairs)


def stage_send(value, stage, row_count):
    base, nxt = stage * row_count, (stage + 1) * row_count
    height = value.shape[1]
    body = send(value, [(base + r, nxt + r) for r in range(row_count)])
    top = send(
        value[:, height - 1 :],
        [(base + r, nxt + r + 1) for r in range(row_count - 1)],
    )
    bottom = send(value[:, :1], [(base + r, nxt + r - 1) for r in range(1, row_count)])
    return body, top, bottom


def local(features, gains, kernels):
    segment_count = lax.axis_size("segment")
    row_count = lax.axis_size("rows")
    segment_index = lax.axis_index("segment")
    frame_count, height, columns, channels = features.shape
    group = frame_count // segment_count
    gain_row = gains[0]
    kernel = kernels[0]
    last_stage = segment_count - 1
    split = frame_count // 2
    if frame_count % 2 == 0 and split >= 2:
        bounds = ((0, split), (split, frame_count))
    else:
        bounds = ((0, frame_count),)

    def straight(source, target):
        return [(source * row_count + r, target * row_count + r) for r in range(row_count)]

    up = [(i, i + 1) for i in range(row_count - 1)]
    down = [(i + 1, i) for i in range(row_count - 1)]
    top = lax.ppermute(features[:, height - 1 :], "rows", up)
    bottom = lax.ppermute(features[:, :1], "rows", down)
    parts = [
        (features[low:high], top[low:high], bottom[low:high]) for low, high in bounds
    ]
    skips = [features[low:high] for low, high in bounds]
    pieces = {}

    for stage in range(segment_count):
        odd = stage % 2 == 1
        final = stage == last_stage
        if stage == last_stage - 1:
            current = jnp.concatenate([body for body, _, _ in parts], axis=0)
            owned = current[stage * group : (stage + 1) * group]
            for target in range(segment_count):
                chunk = current[target * group : (target + 1) * group]
                if stage == 0:
                    owned = jnp.where(segment_index == target, chunk, owned)
                elif target != stage:
                    piece = send(chunk, straight(stage, target))
                    owned = jnp.where(segment_index == target, piece, owned)
        sends_skip = not odd and 0 < stage < last_stage - 1
        history = None
        outputs = []
        for index, ((low, high), (body, above, below)) in enumerate(zip(bounds, parts)):
            activated = activate(jnp.concatenate([above, body, below], axis=1), gain_row)
            if history is None:
                history = jnp.zeros((2,) + activated.shape[1:], activated.dtype)
            window = jnp.concatenate([history, activated], axis=0)
            history = window[-2:]
            convolved = causal_conv(window, kernel, 0).astype(jnp.bfloat16)
            if final:
                for target in range(low // group, high // group):
                    chunk = convolved[target * group - low : (target + 1) * group - low]
                    if target != last_stage:
                        chunk = send(chunk, straight(last_stage, target))
                    pieces[target] = chunk
                continue
            if odd:
                convolved = (skips[index].astype(jnp.float32) + convolved).astype(jnp.bfloat16)
            outputs.append(stage_send(convolved, stage, row_count))
            if sends_skip:
                skips[index] = send(body, straight(stage, stage + 1))
            elif not odd:
                skips[index] = features[low:high]
        parts = outputs

    branch = pieces[0]
    for target in range(1, segment_count):
        branch = jnp.where(segment_index == target, pieces[target], branch)
    return (owned.astype(jnp.float32) + branch.astype(jnp.float32)).astype(jnp.bfloat16)


def solution(mesh):
    placed = (
        P(None, "rows", None, None),
        P("segment", None),
        P("segment", None, None, None, None, None),
    )
    return jax.shard_map(
        local,
        mesh=mesh,
        in_specs=placed,
        out_specs=P("segment", "rows", None, None),
        check_vma=False,
    )
```

```python
import jax
import jax.numpy as jnp
from jax import lax
from jax.sharding import PartitionSpec as P

BOTH = ("segment", "rows")


def activate(values_in, gain_row):
    widened = values_in.astype(jnp.float32)
    mean_square = jnp.mean(widened * widened, axis=-1, keepdims=True)
    return jax.nn.silu(
        widened * lax.rsqrt(mean_square + 1e-06) * gain_row.astype(jnp.float32)
    ).astype(jnp.bfloat16)


def causal_conv(window, kernel, before=2):
    result = lax.conv_general_dilated(
        window[None],
        kernel,
        window_strides=(1, 1, 1),
        padding=((before, 0), (0, 0), (1, 1)),
        dimension_numbers=("NDHWC", "DHWIO", "NDHWC"),
        preferred_element_type=jnp.float32,
    )
    return result[0]


def send(value, pairs):
    return lax.ppermute(value, BOTH, pairs)


def stage_send(value, stage, row_count):
    base, nxt = stage * row_count, (stage + 1) * row_count
    height = value.shape[1]
    body = send(value, [(base + r, nxt + r) for r in range(row_count)])
    top = send(
        value[:, height - 1 :],
        [(base + r, nxt + r + 1) for r in range(row_count - 1)],
    )
    bottom = send(value[:, :1], [(base + r, nxt + r - 1) for r in range(1, row_count)])
    return body, top, bottom


def local(features, gains, kernels):
    segment_count = lax.axis_size("segment")
    row_count = lax.axis_size("rows")
    segment_index = lax.axis_index("segment")
    frame_count, height, columns, channels = features.shape
    group = frame_count // segment_count
    gain_row = gains[0]
    kernel = kernels[0]

    def straight(source, target):
        return [(source * row_count + r, target * row_count + r) for r in range(row_count)]

    up = [(i, i + 1) for i in range(row_count - 1)]
    down = [(i + 1, i) for i in range(row_count - 1)]
    top = lax.ppermute(features[:, height - 1 :], "rows", up)
    bottom = lax.ppermute(features[:, :1], "rows", down)
    current = features
    skip = features
    last_stage = segment_count - 1

    for stage in range(segment_count):
        pieces = [top, current, bottom] if stage else [top, features, bottom]
        window = jnp.concatenate(
            [activate(piece, gain_row) for piece in pieces]
            if stage == 0
            else [activate(jnp.concatenate(pieces, axis=1), gain_row)],
            axis=1,
        )
        odd = stage % 2 == 1
        final = stage == last_stage

        def compute(window, skip, odd=odd, final=final):
            convolved = causal_conv(window, kernel).astype(jnp.bfloat16)
            if odd and not final:
                convolved = (skip.astype(jnp.float32) + convolved).astype(jnp.bfloat16)
            return convolved

        if final:
            activated = jnp.pad(window, ((2, 0), (0, 0), (0, 0), (0, 0)))
            split = (segment_count // 2) * group
            branch = None
            for low, high in ((0, split), (split, frame_count)):
                part = causal_conv(activated[low : high + 2], kernel, 0).astype(jnp.bfloat16)
                for target in range(low // group, high // group):
                    chunk = part[target * group - low : (target + 1) * group - low]
                    if target == last_stage:
                        branch = chunk if branch is None else jnp.where(
                            segment_index == target, chunk, branch
                        )
                    else:
                        piece = send(chunk, straight(last_stage, target))
                        branch = piece if branch is None else jnp.where(
                            segment_index == target, piece, branch
                        )
            break
        produced = compute(window, skip)
        next_skip = current if (not odd and stage > 0 and stage != last_stage - 1) else None
        block_input = current
        current, top, bottom = stage_send(produced, stage, row_count)
        if stage == last_stage - 1:
            after = current[:1, :1, :1, :1].astype(jnp.float32) * 0
            owned = block_input[stage * group : (stage + 1) * group]
            for target in range(segment_count):
                chunk = block_input[target * group : (target + 1) * group]
                if stage == 0:
                    owned = jnp.where(segment_index == target, chunk, owned)
                elif target != stage:
                    tied = (chunk.astype(jnp.float32) + after).astype(jnp.bfloat16)
                    piece = send(tied, straight(stage, target))
                    owned = jnp.where(segment_index == target, piece, owned)
        if next_skip is not None:
            skip = send(next_skip, straight(stage, stage + 1))
        elif not odd:
            skip = features

    return (owned.astype(jnp.float32) + branch.astype(jnp.float32)).astype(jnp.bfloat16)


def solution(mesh):
    placed = (
        P(None, "rows", None, None),
        P("segment", None),
        P("segment", None, None, None, None, None),
    )
    return jax.shard_map(
        local,
        mesh=mesh,
        in_specs=placed,
        out_specs=P("segment", "rows", None, None),
        check_vma=False,
    )
```

```python
import jax
import jax.numpy as jnp
from jax import lax
from jax.sharding import PartitionSpec as P

BOTH = ("segment", "rows")


def activate(values_in, gain_row):
    widened = values_in.astype(jnp.float32)
    mean_square = jnp.mean(widened * widened, axis=-1, keepdims=True)
    return jax.nn.silu(
        widened * lax.rsqrt(mean_square + 1e-06) * gain_row.astype(jnp.float32)
    ).astype(jnp.bfloat16)


def causal_conv(window, kernel, before=2):
    result = lax.conv_general_dilated(
        window[None],
        kernel,
        window_strides=(1, 1, 1),
        padding=((before, 0), (0, 0), (1, 1)),
        dimension_numbers=("NDHWC", "DHWIO", "NDHWC"),
        preferred_element_type=jnp.float32,
    )
    return result[0]


def send(value, pairs):
    return lax.ppermute(value, BOTH, pairs)


def stage_send(value, stage, row_count):
    base, nxt = stage * row_count, (stage + 1) * row_count
    height = value.shape[1]
    body = send(value, [(base + r, nxt + r) for r in range(row_count)])
    top = send(
        value[:, height - 1 :],
        [(base + r, nxt + r + 1) for r in range(row_count - 1)],
    )
    bottom = send(value[:, :1], [(base + r, nxt + r - 1) for r in range(1, row_count)])
    return body, top, bottom


def local(features, gains, kernels):
    segment_count = lax.axis_size("segment")
    row_count = lax.axis_size("rows")
    segment_index = lax.axis_index("segment")
    frame_count, height, columns, channels = features.shape
    group = frame_count // segment_count
    gain_row = gains[0]
    kernel = kernels[0]

    def straight(source, target):
        return [(source * row_count + r, target * row_count + r) for r in range(row_count)]

    up = [(i, i + 1) for i in range(row_count - 1)]
    down = [(i + 1, i) for i in range(row_count - 1)]
    top = lax.ppermute(features[:, height - 1 :], "rows", up)
    bottom = lax.ppermute(features[:, :1], "rows", down)
    current = features
    skip = features
    last_stage = segment_count - 1

    for stage in range(segment_count):
        pieces = [top, current, bottom] if stage else [top, features, bottom]
        window = jnp.concatenate(
            [activate(piece, gain_row) for piece in pieces]
            if stage == 0
            else [activate(jnp.concatenate(pieces, axis=1), gain_row)],
            axis=1,
        )
        odd = stage % 2 == 1
        final = stage == last_stage

        def compute(window, skip, odd=odd, final=final):
            convolved = causal_conv(window, kernel).astype(jnp.bfloat16)
            if odd and not final:
                convolved = (skip.astype(jnp.float32) + convolved).astype(jnp.bfloat16)
            return convolved

        if final:
            activated = jnp.pad(window, ((2, 0), (0, 0), (0, 0), (0, 0)))
            split = (segment_count // 2) * group
            branch = None
            for low, high in ((0, split), (split, frame_count)):
                part = causal_conv(activated[low : high + 2], kernel, 0).astype(jnp.bfloat16)
                for target in range(low // group, high // group):
                    chunk = part[target * group - low : (target + 1) * group - low]
                    if target == last_stage:
                        branch = chunk if branch is None else jnp.where(
                            segment_index == target, chunk, branch
                        )
                    else:
                        piece = send(chunk, straight(last_stage, target))
                        branch = piece if branch is None else jnp.where(
                            segment_index == target, piece, branch
                        )
            break
        produced = compute(window, skip)
        if stage == last_stage - 1:
            owned = current[stage * group : (stage + 1) * group]
            for target in range(segment_count):
                chunk = current[target * group : (target + 1) * group]
                if stage == 0:
                    owned = jnp.where(segment_index == target, chunk, owned)
                elif target != stage:
                    piece = send(chunk, straight(stage, target))
                    owned = jnp.where(segment_index == target, piece, owned)
        next_skip = current if (not odd and stage > 0 and stage != last_stage - 1) else None
        current, top, bottom = stage_send(produced, stage, row_count)
        if next_skip is not None:
            skip = send(next_skip, straight(stage, stage + 1))
        elif not odd:
            skip = features

    return (owned.astype(jnp.float32) + branch.astype(jnp.float32)).astype(jnp.bfloat16)


def solution(mesh):
    placed = (
        P(None, "rows", None, None),
        P("segment", None),
        P("segment", None, None, None, None, None),
    )
    return jax.shard_map(
        local,
        mesh=mesh,
        in_specs=placed,
        out_specs=P("segment", "rows", None, None),
        check_vma=False,
    )
```

```python
import jax
import jax.numpy as jnp
from jax import lax
from jax.sharding import PartitionSpec as P

BOTH = ("segment", "rows")


def activate(values_in, gain_row):
    widened = values_in.astype(jnp.float32)
    mean_square = jnp.mean(widened * widened, axis=-1, keepdims=True)
    return jax.nn.silu(
        widened * lax.rsqrt(mean_square + 1e-06) * gain_row.astype(jnp.float32)
    ).astype(jnp.bfloat16)


def causal_conv(window, kernel, before=2):
    result = lax.conv_general_dilated(
        window[None],
        kernel,
        window_strides=(1, 1, 1),
        padding=((before, 0), (0, 0), (1, 1)),
        dimension_numbers=("NDHWC", "DHWIO", "NDHWC"),
        preferred_element_type=jnp.float32,
    )
    return result[0]


def send(value, pairs):
    return lax.ppermute(value, BOTH, pairs)


def stage_send(value, stage, row_count):
    base, nxt = stage * row_count, (stage + 1) * row_count
    height = value.shape[1]
    body = send(value, [(base + r, nxt + r) for r in range(row_count)])
    top = send(
        value[:, height - 1 :],
        [(base + r, nxt + r + 1) for r in range(row_count - 1)],
    )
    bottom = send(value[:, :1], [(base + r, nxt + r - 1) for r in range(1, row_count)])
    return body, top, bottom


def local(features, gains, kernels):
    segment_count = lax.axis_size("segment")
    row_count = lax.axis_size("rows")
    segment_index = lax.axis_index("segment")
    frame_count, height, columns, channels = features.shape
    group = frame_count // segment_count
    gain_row = gains[0]
    kernel = kernels[0]

    def straight(source, target):
        return [(source * row_count + r, target * row_count + r) for r in range(row_count)]

    up = [(i, i + 1) for i in range(row_count - 1)]
    down = [(i + 1, i) for i in range(row_count - 1)]
    top = lax.ppermute(features[:, height - 1 :], "rows", up)
    bottom = lax.ppermute(features[:, :1], "rows", down)
    current = features
    skip = features
    last_stage = segment_count - 1

    for stage in range(segment_count):
        pieces = [top, current, bottom] if stage else [top, features, bottom]
        window = jnp.concatenate(
            [activate(piece, gain_row) for piece in pieces]
            if stage == 0
            else [activate(jnp.concatenate(pieces, axis=1), gain_row)],
            axis=1,
        )
        odd = stage % 2 == 1
        final = stage == last_stage

        def compute(window, skip, odd=odd, final=final):
            convolved = causal_conv(window, kernel).astype(jnp.bfloat16)
            if odd and not final:
                convolved = (skip.astype(jnp.float32) + convolved).astype(jnp.bfloat16)
            return convolved

        if final:
            activated = jnp.pad(window, ((2, 0), (0, 0), (0, 0), (0, 0)))
            split = last_stage * group
            branch = None
            for low, high in ((0, split), (split, frame_count)) if split else ((0, frame_count),):
                part = causal_conv(activated[low : high + 2], kernel, 0).astype(jnp.bfloat16)
                for target in range(low // group, high // group):
                    chunk = part[target * group - low : (target + 1) * group - low]
                    if target == last_stage:
                        branch = chunk if branch is None else jnp.where(
                            segment_index == target, chunk, branch
                        )
                    else:
                        piece = send(chunk, straight(last_stage, target))
                        branch = piece if branch is None else jnp.where(
                            segment_index == target, piece, branch
                        )
            break
        produced = compute(window, skip)
        if stage == last_stage - 1:
            owned = current[stage * group : (stage + 1) * group]
            for target in range(segment_count):
                chunk = current[target * group : (target + 1) * group]
                if stage == 0:
                    owned = jnp.where(segment_index == target, chunk, owned)
                elif target != stage:
                    piece = send(chunk, straight(stage, target))
                    owned = jnp.where(segment_index == target, piece, owned)
        next_skip = current if (not odd and stage > 0 and stage != last_stage - 1) else None
        current, top, bottom = stage_send(produced, stage, row_count)
        if next_skip is not None:
            skip = send(next_skip, straight(stage, stage + 1))
        elif not odd:
            skip = features

    return (owned.astype(jnp.float32) + branch.astype(jnp.float32)).astype(jnp.bfloat16)


def solution(mesh):
    placed = (
        P(None, "rows", None, None),
        P("segment", None),
        P("segment", None, None, None, None, None),
    )
    return jax.shard_map(
        local,
        mesh=mesh,
        in_specs=placed,
        out_specs=P("segment", "rows", None, None),
        check_vma=False,
    )
```

```python
import jax
import jax.numpy as jnp
from jax import lax
from jax.sharding import PartitionSpec as P

BOTH = ("segment", "rows")


def activate(values_in, gain_row):
    widened = values_in.astype(jnp.float32)
    mean_square = jnp.mean(widened * widened, axis=-1, keepdims=True)
    return jax.nn.silu(
        widened * lax.rsqrt(mean_square + 1e-06) * gain_row.astype(jnp.float32)
    ).astype(jnp.bfloat16)


def causal_conv(window, kernel, before=2):
    result = lax.conv_general_dilated(
        window[None],
        kernel,
        window_strides=(1, 1, 1),
        padding=((before, 0), (0, 0), (1, 1)),
        dimension_numbers=("NDHWC", "DHWIO", "NDHWC"),
        preferred_element_type=jnp.float32,
    )
    return result[0]


def send(value, pairs):
    return lax.ppermute(value, BOTH, pairs)


def stage_send(value, stage, row_count):
    base, nxt = stage * row_count, (stage + 1) * row_count
    height = value.shape[1]
    body = send(value, [(base + r, nxt + r) for r in range(row_count)])
    top = send(
        value[:, height - 1 :],
        [(base + r, nxt + r + 1) for r in range(row_count - 1)],
    )
    bottom = send(value[:, :1], [(base + r, nxt + r - 1) for r in range(1, row_count)])
    return body, top, bottom


def local(features, gains, kernels):
    segment_count = lax.axis_size("segment")
    row_count = lax.axis_size("rows")
    segment_index = lax.axis_index("segment")
    frame_count, height, columns, channels = features.shape
    group = frame_count // segment_count
    gain_row = gains[0]
    kernel = kernels[0]

    def straight(source, target):
        return [(source * row_count + r, target * row_count + r) for r in range(row_count)]

    up = [(i, i + 1) for i in range(row_count - 1)]
    down = [(i + 1, i) for i in range(row_count - 1)]
    top = lax.ppermute(features[:, height - 1 :], "rows", up)
    bottom = lax.ppermute(features[:, :1], "rows", down)
    current = features
    skip = features
    last_stage = segment_count - 1

    for stage in range(segment_count):
        pieces = [top, current, bottom] if stage else [top, features, bottom]
        window = jnp.concatenate(
            [activate(piece, gain_row) for piece in pieces]
            if stage == 0
            else [activate(jnp.concatenate(pieces, axis=1), gain_row)],
            axis=1,
        )
        odd = stage % 2 == 1
        final = stage == last_stage

        def compute(window, skip, odd=odd, final=final):
            convolved = causal_conv(window, kernel).astype(jnp.bfloat16)
            if odd and not final:
                convolved = (skip.astype(jnp.float32) + convolved).astype(jnp.bfloat16)
            return convolved

        if final:
            activated = jnp.pad(window, ((2, 0), (0, 0), (0, 0), (0, 0)))
            split = (segment_count // 2) * group
            branch = None
            for low, high in ((split, frame_count), (0, split)):
                part = causal_conv(activated[low : high + 2], kernel, 0).astype(jnp.bfloat16)
                for target in range(low // group, high // group):
                    chunk = part[target * group - low : (target + 1) * group - low]
                    if target == last_stage:
                        branch = chunk if branch is None else jnp.where(
                            segment_index == target, chunk, branch
                        )
                    else:
                        piece = send(chunk, straight(last_stage, target))
                        branch = piece if branch is None else jnp.where(
                            segment_index == target, piece, branch
                        )
            break
        produced = compute(window, skip)
        if stage == last_stage - 1:
            owned = current[stage * group : (stage + 1) * group]
            for target in range(segment_count):
                chunk = current[target * group : (target + 1) * group]
                if stage == 0:
                    owned = jnp.where(segment_index == target, chunk, owned)
                elif target != stage:
                    piece = send(chunk, straight(stage, target))
                    owned = jnp.where(segment_index == target, piece, owned)
        next_skip = current if (not odd and stage > 0 and stage != last_stage - 1) else None
        current, top, bottom = stage_send(produced, stage, row_count)
        if next_skip is not None:
            skip = send(next_skip, straight(stage, stage + 1))
        elif not odd:
            skip = features

    return (owned.astype(jnp.float32) + branch.astype(jnp.float32)).astype(jnp.bfloat16)


def solution(mesh):
    placed = (
        P(None, "rows", None, None),
        P("segment", None),
        P("segment", None, None, None, None, None),
    )
    return jax.shard_map(
        local,
        mesh=mesh,
        in_specs=placed,
        out_specs=P("segment", "rows", None, None),
        check_vma=False,
    )
```

```python
import jax
import jax.numpy as jnp
from jax import lax
from jax.sharding import PartitionSpec as P

BOTH = ("segment", "rows")


def activate(values_in, gain_row):
    widened = values_in.astype(jnp.float32)
    mean_square = jnp.mean(widened * widened, axis=-1, keepdims=True)
    return jax.nn.silu(
        widened * lax.rsqrt(mean_square + 1e-06) * gain_row.astype(jnp.float32)
    ).astype(jnp.bfloat16)


def causal_conv(window, kernel, before=2):
    return batched_conv(window[None], kernel, before)[0]


def batched_conv(windows, kernel, before=2):
    return lax.conv_general_dilated(
        windows,
        kernel,
        window_strides=(1, 1, 1),
        padding=((before, 0), (0, 0), (1, 1)),
        dimension_numbers=("NDHWC", "DHWIO", "NDHWC"),
        preferred_element_type=jnp.float32,
    )


def send(value, pairs):
    return lax.ppermute(value, BOTH, pairs)


def stage_send(value, stage, row_count, edges_after=False):
    base, nxt = stage * row_count, (stage + 1) * row_count
    height = value.shape[1]
    body = send(value, [(base + r, nxt + r) for r in range(row_count)])
    if edges_after:
        tie = body[:1, :1, :1, :1].astype(jnp.float32) * 0
        value = (value.astype(jnp.float32) + tie).astype(jnp.bfloat16)
    top = send(
        value[:, height - 1 :],
        [(base + r, nxt + r + 1) for r in range(row_count - 1)],
    )
    bottom = send(value[:, :1], [(base + r, nxt + r - 1) for r in range(1, row_count)])
    return body, top, bottom


def local(features, gains, kernels):
    segment_count = lax.axis_size("segment")
    row_count = lax.axis_size("rows")
    segment_index = lax.axis_index("segment")
    frame_count, height, columns, channels = features.shape
    group = frame_count // segment_count
    gain_row = gains[0]
    kernel = kernels[0]

    def straight(source, target):
        return [(source * row_count + r, target * row_count + r) for r in range(row_count)]

    up = [(i, i + 1) for i in range(row_count - 1)]
    down = [(i + 1, i) for i in range(row_count - 1)]
    top = lax.ppermute(features[:, height - 1 :], "rows", up)
    bottom = lax.ppermute(features[:, :1], "rows", down)
    current = features
    skip = features
    last_stage = segment_count - 1
    split_rows = True

    for stage in range(segment_count):
        pieces = [top, current, bottom] if stage else [top, features, bottom]
        window = jnp.concatenate(
            [activate(piece, gain_row) for piece in pieces]
            if stage == 0
            else [activate(jnp.concatenate(pieces, axis=1), gain_row)],
            axis=1,
        )
        odd = stage % 2 == 1
        final = stage == last_stage

        def compute(window, skip, odd=odd, final=final):
            convolved = causal_conv(window, kernel).astype(jnp.bfloat16)
            if odd and not final:
                convolved = (skip.astype(jnp.float32) + convolved).astype(jnp.bfloat16)
            return convolved

        if final:
            activated = jnp.pad(window, ((2, 0), (0, 0), (0, 0), (0, 0)))
            split = (segment_count // 2) * group
            branch = None
            for low, high in ((0, split), (split, frame_count)):
                part = causal_conv(activated[low : high + 2], kernel, 0).astype(jnp.bfloat16)
                for target in range(low // group, high // group):
                    chunk = part[target * group - low : (target + 1) * group - low]
                    if target == last_stage:
                        branch = chunk if branch is None else jnp.where(
                            segment_index == target, chunk, branch
                        )
                    else:
                        piece = send(chunk, straight(last_stage, target))
                        branch = piece if branch is None else jnp.where(
                            segment_index == target, piece, branch
                        )
            break
        if 0 < stage < last_stage and height >= 3 and split_rows:
            inner = activate(current, gain_row)
            middle = causal_conv(inner, kernel)
            edges = jnp.stack(
                [
                    jnp.concatenate([activate(top, gain_row), inner[:, :2]], axis=1),
                    jnp.concatenate([inner[:, height - 2 :], activate(bottom, gain_row)], axis=1),
                ]
            )
            rims = batched_conv(edges, kernel)
            convolved = jnp.concatenate([rims[0], middle, rims[1]], axis=1).astype(jnp.bfloat16)
            if odd:
                convolved = (skip.astype(jnp.float32) + convolved).astype(jnp.bfloat16)
            produced = convolved
        else:
            produced = compute(window, skip)
        if stage == last_stage - 1:
            owned = current[stage * group : (stage + 1) * group]
            for target in range(segment_count):
                chunk = current[target * group : (target + 1) * group]
                if stage == 0:
                    owned = jnp.where(segment_index == target, chunk, owned)
                elif target != stage:
                    piece = send(chunk, straight(stage, target))
                    owned = jnp.where(segment_index == target, piece, owned)
        next_skip = current if (not odd and stage > 0 and stage != last_stage - 1) else None
        current, top, bottom = stage_send(
            produced, stage, row_count, split_rows and height >= 3 and stage + 1 < last_stage
        )
        if next_skip is not None:
            skip = send(next_skip, straight(stage, stage + 1))
        elif not odd:
            skip = features

    return (owned.astype(jnp.float32) + branch.astype(jnp.float32)).astype(jnp.bfloat16)


def solution(mesh):
    placed = (
        P(None, "rows", None, None),
        P("segment", None),
        P("segment", None, None, None, None, None),
    )
    return jax.shard_map(
        local,
        mesh=mesh,
        in_specs=placed,
        out_specs=P("segment", "rows", None, None),
        check_vma=False,
    )
```

```python
import jax
import jax.numpy as jnp
from jax import lax
from jax.sharding import PartitionSpec as P

BOTH = ("segment", "rows")


def activate(values_in, gain_row):
    widened = values_in.astype(jnp.float32)
    mean_square = jnp.mean(widened * widened, axis=-1, keepdims=True)
    return jax.nn.silu(
        widened * lax.rsqrt(mean_square + 1e-06) * gain_row.astype(jnp.float32)
    ).astype(jnp.bfloat16)


def causal_conv(window, kernel, before=2):
    result = lax.conv_general_dilated(
        window[None],
        kernel,
        window_strides=(1, 1, 1),
        padding=((before, 0), (0, 0), (1, 1)),
        dimension_numbers=("NDHWC", "DHWIO", "NDHWC"),
        preferred_element_type=jnp.float32,
    )
    return result[0]


def send(value, pairs):
    return lax.ppermute(value, BOTH, pairs)


def stage_send(value, stage, row_count):
    base, nxt = stage * row_count, (stage + 1) * row_count
    height = value.shape[1]
    body = send(value, [(base + r, nxt + r) for r in range(row_count)])
    top = send(
        value[:, height - 1 :],
        [(base + r, nxt + r + 1) for r in range(row_count - 1)],
    )
    bottom = send(value[:, :1], [(base + r, nxt + r - 1) for r in range(1, row_count)])
    return body, top, bottom


def local(features, gains, kernels):
    segment_count = lax.axis_size("segment")
    row_count = lax.axis_size("rows")
    segment_index = lax.axis_index("segment")
    frame_count, height, columns, channels = features.shape
    group = frame_count // segment_count
    gain_row = gains[0]
    kernel = kernels[0]

    def straight(source, target):
        return [(source * row_count + r, target * row_count + r) for r in range(row_count)]

    up = [(i, i + 1) for i in range(row_count - 1)]
    down = [(i + 1, i) for i in range(row_count - 1)]
    top = lax.ppermute(features[:, height - 1 :], "rows", up)
    bottom = lax.ppermute(features[:, :1], "rows", down)
    current = features
    skip = features
    last_stage = segment_count - 1
    early = {}

    for stage in range(segment_count):
        pieces = [top, current, bottom] if stage else [top, features, bottom]
        window = jnp.concatenate(
            [activate(piece, gain_row) for piece in pieces]
            if stage == 0
            else [activate(jnp.concatenate(pieces, axis=1), gain_row)],
            axis=1,
        )
        odd = stage % 2 == 1
        final = stage == last_stage

        def compute(window, skip, odd=odd, final=final):
            convolved = causal_conv(window, kernel).astype(jnp.bfloat16)
            if odd and not final:
                convolved = (skip.astype(jnp.float32) + convolved).astype(jnp.bfloat16)
            return convolved

        if final:
            activated = jnp.pad(window, ((2, 0), (0, 0), (0, 0), (0, 0)))
            split = (segment_count // 2) * group
            branch = None
            for low, high in ((0, split), (split, frame_count)):
                part = causal_conv(activated[low : high + 2], kernel, 0).astype(jnp.bfloat16)
                for target in range(low // group, high // group):
                    chunk = part[target * group - low : (target + 1) * group - low]
                    if target == last_stage:
                        branch = chunk if branch is None else jnp.where(
                            segment_index == target, chunk, branch
                        )
                    else:
                        piece = send(chunk, straight(last_stage, target))
                        branch = piece if branch is None else jnp.where(
                            segment_index == target, piece, branch
                        )
            break
        produced = compute(window, skip)
        if stage == last_stage - 2:
            early = {}
            for target in range(stage + 1):
                chunk = produced[target * group : (target + 1) * group]
                early[target] = chunk if target == stage else send(chunk, straight(stage, target))
        if stage == last_stage - 1:
            owned = current[stage * group : (stage + 1) * group]
            for target in range(segment_count):
                chunk = current[target * group : (target + 1) * group]
                if stage == 0:
                    owned = jnp.where(segment_index == target, chunk, owned)
                elif target in early:
                    owned = jnp.where(segment_index == target, early[target], owned)
                elif target != stage:
                    piece = send(chunk, straight(stage, target))
                    owned = jnp.where(segment_index == target, piece, owned)
        next_skip = current if (not odd and stage > 0 and stage != last_stage - 1) else None
        current, top, bottom = stage_send(produced, stage, row_count)
        if next_skip is not None:
            skip = send(next_skip, straight(stage, stage + 1))
        elif not odd:
            skip = features

    return (owned.astype(jnp.float32) + branch.astype(jnp.float32)).astype(jnp.bfloat16)


def solution(mesh):
    placed = (
        P(None, "rows", None, None),
        P("segment", None),
        P("segment", None, None, None, None, None),
    )
    return jax.shard_map(
        local,
        mesh=mesh,
        in_specs=placed,
        out_specs=P("segment", "rows", None, None),
        check_vma=False,
    )
```

```python
import jax
import jax.numpy as jnp
from jax import lax
from jax.sharding import PartitionSpec as P

BOTH = ("segment", "rows")


def activate(values_in, gain_row):
    widened = values_in.astype(jnp.float32)
    mean_square = jnp.mean(widened * widened, axis=-1, keepdims=True)
    return jax.nn.silu(
        widened * lax.rsqrt(mean_square + 1e-06) * gain_row.astype(jnp.float32)
    ).astype(jnp.bfloat16)


def causal_conv(window, kernel, before=2):
    result = lax.conv_general_dilated(
        window[None],
        kernel,
        window_strides=(1, 1, 1),
        padding=((before, 0), (0, 0), (1, 1)),
        dimension_numbers=("NDHWC", "DHWIO", "NDHWC"),
        preferred_element_type=jnp.float32,
    )
    return result[0]


def send(value, pairs):
    return lax.ppermute(value, BOTH, pairs)


def stage_send(value, stage, row_count):
    base, nxt = stage * row_count, (stage + 1) * row_count
    height = value.shape[1]
    body = send(value, [(base + r, nxt + r) for r in range(row_count)])
    top = send(
        value[:, height - 1 :],
        [(base + r, nxt + r + 1) for r in range(row_count - 1)],
    )
    bottom = send(value[:, :1], [(base + r, nxt + r - 1) for r in range(1, row_count)])
    return body, top, bottom


def local(features, gains, kernels):
    segment_count = lax.axis_size("segment")
    row_count = lax.axis_size("rows")
    segment_index = lax.axis_index("segment")
    frame_count, height, columns, channels = features.shape
    group = frame_count // segment_count
    gain_row = gains[0]
    kernel = kernels[0]

    def straight(source, target):
        return [(source * row_count + r, target * row_count + r) for r in range(row_count)]

    up = [(i, i + 1) for i in range(row_count - 1)]
    down = [(i + 1, i) for i in range(row_count - 1)]
    top = send(features[:, height - 1 :], up)
    bottom = send(features[:, :1], down)
    current = features
    skip = features
    last_stage = segment_count - 1

    for stage in range(segment_count):
        pieces = [top, current, bottom] if stage else [top, features, bottom]
        window = jnp.concatenate(
            [activate(piece, gain_row) for piece in pieces]
            if stage == 0
            else [activate(jnp.concatenate(pieces, axis=1), gain_row)],
            axis=1,
        )
        odd = stage % 2 == 1
        final = stage == last_stage

        def compute(window, skip, odd=odd, final=final):
            convolved = causal_conv(window, kernel).astype(jnp.bfloat16)
            if odd and not final:
                convolved = (skip.astype(jnp.float32) + convolved).astype(jnp.bfloat16)
            return convolved

        if final:
            activated = jnp.pad(window, ((2, 0), (0, 0), (0, 0), (0, 0)))
            split = (segment_count // 2) * group
            branch = None
            for low, high in ((0, split), (split, frame_count)):
                part = causal_conv(activated[low : high + 2], kernel, 0).astype(jnp.bfloat16)
                for target in range(low // group, high // group):
                    chunk = part[target * group - low : (target + 1) * group - low]
                    if target == last_stage:
                        branch = chunk if branch is None else jnp.where(
                            segment_index == target, chunk, branch
                        )
                    else:
                        piece = send(chunk, straight(last_stage, target))
                        branch = piece if branch is None else jnp.where(
                            segment_index == target, piece, branch
                        )
            break
        produced = compute(window, skip)
        if stage == last_stage - 1:
            owned = current[stage * group : (stage + 1) * group]
            for target in range(segment_count):
                chunk = current[target * group : (target + 1) * group]
                if stage == 0:
                    owned = jnp.where(segment_index == target, chunk, owned)
                elif target != stage:
                    piece = send(chunk, straight(stage, target))
                    owned = jnp.where(segment_index == target, piece, owned)
        next_skip = current if (not odd and stage > 0 and stage != last_stage - 1) else None
        current, top, bottom = stage_send(produced, stage, row_count)
        if next_skip is not None:
            skip = send(next_skip, straight(stage, stage + 1))
        elif not odd:
            skip = features

    return (owned.astype(jnp.float32) + branch.astype(jnp.float32)).astype(jnp.bfloat16)


def solution(mesh):
    placed = (
        P(None, "rows", None, None),
        P("segment", None),
        P("segment", None, None, None, None, None),
    )
    return jax.shard_map(
        local,
        mesh=mesh,
        in_specs=placed,
        out_specs=P("segment", "rows", None, None),
        check_vma=False,
    )
```

```python
import jax
import jax.numpy as jnp
from jax import lax
from jax.sharding import PartitionSpec as P

BOTH = ("segment", "rows")


def activate(values_in, gain_row):
    widened = values_in.astype(jnp.float32)
    mean_square = jnp.mean(widened * widened, axis=-1, keepdims=True)
    return jax.nn.silu(
        widened * lax.rsqrt(mean_square + 1e-06) * gain_row.astype(jnp.float32)
    ).astype(jnp.bfloat16)


def causal_conv(window, kernel, before=2):
    result = lax.conv_general_dilated(
        window[None],
        kernel,
        window_strides=(1, 1, 1),
        padding=((before, 0), (0, 0), (1, 1)),
        dimension_numbers=("NDHWC", "DHWIO", "NDHWC"),
        preferred_element_type=jnp.float32,
    )
    return result[0]


def send(value, pairs):
    return lax.ppermute(value, BOTH, pairs)


def stage_send(value, stage, row_count):
    base, nxt = stage * row_count, (stage + 1) * row_count
    height = value.shape[1]
    body = send(value, [(base + r, nxt + r) for r in range(row_count)])
    top = send(
        value[:, height - 1 :],
        [(base + r, nxt + r + 1) for r in range(row_count - 1)],
    )
    bottom = send(value[:, :1], [(base + r, nxt + r - 1) for r in range(1, row_count)])
    return body, top, bottom


def local(features, gains, kernels):
    segment_count = lax.axis_size("segment")
    row_count = lax.axis_size("rows")
    segment_index = lax.axis_index("segment")
    frame_count, height, columns, channels = features.shape
    group = frame_count // segment_count
    gain_row = gains[0]
    kernel = kernels[0]

    def straight(source, target):
        return [(source * row_count + r, target * row_count + r) for r in range(row_count)]

    up = [(i, i + 1) for i in range(row_count - 1)]
    down = [(i + 1, i) for i in range(row_count - 1)]
    top = send(features[:, height - 1 :], up)
    bottom = send(features[:, :1], down)
    current = features
    skip = features
    last_stage = segment_count - 1

    for stage in range(segment_count):
        pieces = [top, current, bottom] if stage else [top, features, bottom]
        window = jnp.concatenate(
            [activate(piece, gain_row) for piece in pieces]
            if stage == 0
            else [activate(jnp.concatenate(pieces, axis=1), gain_row)],
            axis=1,
        )
        odd = stage % 2 == 1
        final = stage == last_stage

        def compute(window, skip, odd=odd, final=final):
            convolved = causal_conv(window, kernel).astype(jnp.bfloat16)
            if odd and not final:
                convolved = (skip.astype(jnp.float32) + convolved).astype(jnp.bfloat16)
            return convolved

        if final:
            activated = jnp.pad(window, ((2, 0), (0, 0), (0, 0), (0, 0)))
            split = (segment_count // 2) * group
            branch = None
            own_start = frame_count - group
            bounds = [(0, split), (split, own_start), (own_start, frame_count)]
            for low, high in [(a, b) for a, b in bounds if b > a]:
                part = causal_conv(activated[low : high + 2], kernel, 0).astype(jnp.bfloat16)
                for target in range(low // group, high // group):
                    chunk = part[target * group - low : (target + 1) * group - low]
                    if target == last_stage:
                        branch = chunk if branch is None else jnp.where(
                            segment_index == target, chunk, branch
                        )
                    else:
                        piece = send(chunk, straight(last_stage, target))
                        branch = piece if branch is None else jnp.where(
                            segment_index == target, piece, branch
                        )
            break
        produced = compute(window, skip)
        if stage == last_stage - 1:
            owned = current[stage * group : (stage + 1) * group]
            for target in range(segment_count):
                chunk = current[target * group : (target + 1) * group]
                if stage == 0:
                    owned = jnp.where(segment_index == target, chunk, owned)
                elif target != stage:
                    piece = send(chunk, straight(stage, target))
                    owned = jnp.where(segment_index == target, piece, owned)
        next_skip = current if (not odd and stage > 0 and stage != last_stage - 1) else None
        current, top, bottom = stage_send(produced, stage, row_count)
        if next_skip is not None:
            skip = send(next_skip, straight(stage, stage + 1))
        elif not odd:
            skip = features

    return (owned.astype(jnp.float32) + branch.astype(jnp.float32)).astype(jnp.bfloat16)


def solution(mesh):
    placed = (
        P(None, "rows", None, None),
        P("segment", None),
        P("segment", None, None, None, None, None),
    )
    return jax.shard_map(
        local,
        mesh=mesh,
        in_specs=placed,
        out_specs=P("segment", "rows", None, None),
        check_vma=False,
    )
```

```python
import jax
import jax.numpy as jnp
from jax import lax
from jax.sharding import PartitionSpec as P

BOTH = ("segment", "rows")


def activate(values_in, gain_row):
    widened = values_in.astype(jnp.float32)
    mean_square = jnp.mean(widened * widened, axis=-1, keepdims=True)
    return jax.nn.silu(
        widened * lax.rsqrt(mean_square + 1e-06) * gain_row.astype(jnp.float32)
    ).astype(jnp.bfloat16)


def causal_conv(window, kernel, before=2):
    result = lax.conv_general_dilated(
        window[None],
        kernel,
        window_strides=(1, 1, 1),
        padding=((before, 0), (0, 0), (1, 1)),
        dimension_numbers=("NDHWC", "DHWIO", "NDHWC"),
        preferred_element_type=jnp.float32,
    )
    return result[0]


def send(value, pairs):
    return lax.ppermute(value, BOTH, pairs)


def stage_send(value, stage, row_count):
    base, nxt = stage * row_count, (stage + 1) * row_count
    height = value.shape[1]
    body = send(value, [(base + r, nxt + r) for r in range(row_count)])
    top = send(
        value[:, height - 1 :],
        [(base + r, nxt + r + 1) for r in range(row_count - 1)],
    )
    bottom = send(value[:, :1], [(base + r, nxt + r - 1) for r in range(1, row_count)])
    return body, top, bottom


def local(features, gains, kernels):
    segment_count = lax.axis_size("segment")
    row_count = lax.axis_size("rows")
    segment_index = lax.axis_index("segment")
    frame_count, height, columns, channels = features.shape
    group = frame_count // segment_count
    gain_row = gains[0]
    kernel = kernels[0]

    def straight(source, target):
        return [(source * row_count + r, target * row_count + r) for r in range(row_count)]

    up = [(i, i + 1) for i in range(row_count - 1)]
    down = [(i + 1, i) for i in range(row_count - 1)]
    top = send(features[:, height - 1 :], up)
    bottom = send(features[:, :1], down)
    current = features
    skip = features
    last_stage = segment_count - 1
    early = {}

    for stage in range(segment_count):
        pieces = [top, current, bottom] if stage else [top, features, bottom]
        window = jnp.concatenate(
            [activate(piece, gain_row) for piece in pieces]
            if stage == 0
            else [activate(jnp.concatenate(pieces, axis=1), gain_row)],
            axis=1,
        )
        odd = stage % 2 == 1
        final = stage == last_stage

        def compute(window, skip, odd=odd, final=final):
            convolved = causal_conv(window, kernel).astype(jnp.bfloat16)
            if odd and not final:
                convolved = (skip.astype(jnp.float32) + convolved).astype(jnp.bfloat16)
            return convolved

        if final:
            activated = jnp.pad(window, ((2, 0), (0, 0), (0, 0), (0, 0)))
            split = (segment_count // 2) * group
            branch = None
            for low, high in ((0, split), (split, frame_count)):
                part = causal_conv(activated[low : high + 2], kernel, 0).astype(jnp.bfloat16)
                for target in range(low // group, high // group):
                    chunk = part[target * group - low : (target + 1) * group - low]
                    if target == last_stage:
                        branch = chunk if branch is None else jnp.where(
                            segment_index == target, chunk, branch
                        )
                    else:
                        piece = send(chunk, straight(last_stage, target))
                        branch = piece if branch is None else jnp.where(
                            segment_index == target, piece, branch
                        )
            break
        produced = compute(window, skip)
        if stage == last_stage - 2:
            early = {}
            for target in range(stage + 1):
                chunk = produced[target * group : (target + 1) * group]
                early[target] = chunk if target == stage else send(chunk, straight(stage, target))
        if stage == last_stage - 1:
            owned = current[stage * group : (stage + 1) * group]
            for target in range(segment_count):
                chunk = current[target * group : (target + 1) * group]
                if stage == 0:
                    owned = jnp.where(segment_index == target, chunk, owned)
                elif target in early:
                    owned = jnp.where(segment_index == target, early[target], owned)
                elif target != stage:
                    piece = send(chunk, straight(stage, target))
                    owned = jnp.where(segment_index == target, piece, owned)
        next_skip = current if (not odd and stage > 0 and stage != last_stage - 1) else None
        current, top, bottom = stage_send(produced, stage, row_count)
        if next_skip is not None:
            skip = send(next_skip, straight(stage, stage + 1))
        elif not odd:
            skip = features

    return (owned.astype(jnp.float32) + branch.astype(jnp.float32)).astype(jnp.bfloat16)


def solution(mesh):
    placed = (
        P(None, "rows", None, None),
        P("segment", None),
        P("segment", None, None, None, None, None),
    )
    return jax.shard_map(
        local,
        mesh=mesh,
        in_specs=placed,
        out_specs=P("segment", "rows", None, None),
        check_vma=False,
    )
```

```python
import jax
import jax.numpy as jnp
from jax import lax
from jax.sharding import PartitionSpec as P

BOTH = ("segment", "rows")


def activate(values_in, gain_row):
    widened = values_in.astype(jnp.float32)
    mean_square = jnp.mean(widened * widened, axis=-1, keepdims=True)
    return jax.nn.silu(
        widened * lax.rsqrt(mean_square + 1e-06) * gain_row.astype(jnp.float32)
    ).astype(jnp.bfloat16)


def causal_conv(window, kernel, before=2):
    result = lax.conv_general_dilated(
        window[None],
        kernel,
        window_strides=(1, 1, 1),
        padding=((before, 0), (0, 0), (1, 1)),
        dimension_numbers=("NDHWC", "DHWIO", "NDHWC"),
        preferred_element_type=jnp.float32,
    )
    return result[0]


def send(value, pairs):
    return lax.ppermute(value, BOTH, pairs)


def stage_send(value, stage, row_count):
    base, nxt = stage * row_count, (stage + 1) * row_count
    height = value.shape[1]
    body = send(value, [(base + r, nxt + r) for r in range(row_count)])
    top = send(
        value[:, height - 1 :],
        [(base + r, nxt + r + 1) for r in range(row_count - 1)],
    )
    bottom = send(value[:, :1], [(base + r, nxt + r - 1) for r in range(1, row_count)])
    return body, top, bottom


def local(features, gains, kernels):
    segment_count = lax.axis_size("segment")
    row_count = lax.axis_size("rows")
    segment_index = lax.axis_index("segment")
    frame_count, height, columns, channels = features.shape
    group = frame_count // segment_count
    gain_row = gains[0]
    kernel = kernels[0]

    def straight(source, target):
        return [(source * row_count + r, target * row_count + r) for r in range(row_count)]

    up = [(i, i + 1) for i in range(row_count - 1)]
    down = [(i + 1, i) for i in range(row_count - 1)]
    top = send(features[:, height - 1 :], up)
    bottom = send(features[:, :1], down)
    current = features
    skip = features
    last_stage = segment_count - 1

    for stage in range(segment_count):
        pieces = [top, current, bottom] if stage else [top, features, bottom]
        window = jnp.concatenate([activate(piece, gain_row) for piece in pieces], axis=1)
        odd = stage % 2 == 1
        final = stage == last_stage

        def compute(window, skip, odd=odd, final=final):
            convolved = causal_conv(window, kernel).astype(jnp.bfloat16)
            if odd and not final:
                convolved = (skip.astype(jnp.float32) + convolved).astype(jnp.bfloat16)
            return convolved

        if final:
            activated = jnp.pad(window, ((2, 0), (0, 0), (0, 0), (0, 0)))
            split = (segment_count // 2) * group
            branch = None
            for low, high in ((0, split), (split, frame_count)):
                part = causal_conv(activated[low : high + 2], kernel, 0).astype(jnp.bfloat16)
                for target in range(low // group, high // group):
                    chunk = part[target * group - low : (target + 1) * group - low]
                    if target == last_stage:
                        branch = chunk if branch is None else jnp.where(
                            segment_index == target, chunk, branch
                        )
                    else:
                        piece = send(chunk, straight(last_stage, target))
                        branch = piece if branch is None else jnp.where(
                            segment_index == target, piece, branch
                        )
            break
        produced = compute(window, skip)
        if stage == last_stage - 1:
            owned = current[stage * group : (stage + 1) * group]
            for target in range(segment_count):
                chunk = current[target * group : (target + 1) * group]
                if stage == 0:
                    owned = jnp.where(segment_index == target, chunk, owned)
                elif target != stage:
                    piece = send(chunk, straight(stage, target))
                    owned = jnp.where(segment_index == target, piece, owned)
        next_skip = current if (not odd and stage > 0 and stage != last_stage - 1) else None
        current, top, bottom = stage_send(produced, stage, row_count)
        if next_skip is not None:
            skip = send(next_skip, straight(stage, stage + 1))
        elif not odd:
            skip = features

    return (owned.astype(jnp.float32) + branch.astype(jnp.float32)).astype(jnp.bfloat16)


def solution(mesh):
    placed = (
        P(None, "rows", None, None),
        P("segment", None),
        P("segment", None, None, None, None, None),
    )
    return jax.shard_map(
        local,
        mesh=mesh,
        in_specs=placed,
        out_specs=P("segment", "rows", None, None),
        check_vma=False,
    )
```
